512 devices in a mesh: section: 16 (over x_hi, y), dp: 8 (over z), mp: 4 (over x_lo, core).
Axes of the slice: x: 4 (x_hi: 2, x_lo: 2; x = x_hi * 2 + x_lo), y: 8, z: 8, core: 2. Of those that a mesh axis runs over, the one named last changes fastest.
Arguments:
- cotangent: bfloat16 [1024, 4096], P('dp', 'mp'), may hold values from -6 to 6
- saved_inputs: bfloat16 [16, 1024, 4096], P('section', 'dp', 'mp'), may hold values from -6 to 6
- pre_acts: bfloat16 [16, 1024, 4096], P('section', 'dp', 'mp'), may hold values from -8 to 8
- weights: bfloat16 [16, 4096, 4096], P('section', 'mp', 'dp'), may hold values from -0.046875 to 0.046875
- proj_in: bfloat16 [16, 4096, 64], P('section', 'mp'), may hold values from -0.09375 to 0.09375
- proj_out: bfloat16 [16, 4096, 64], P('section', 'mp'), may hold values from -0.09375 to 0.09375
- query_panels: float32 [16, 16, 4096], P('section', 'dp', 'mp'), may hold values from -4 to 4
- partners: int32 [8, 8], replicated, may hold values from 0 to 7, as said below
Outputs:
- train_panels: float32 [16, 32, 4096], P('section', 'dp', 'mp')
- scores: float32 [16, 8, 4], replicated
The draws below stay inside these ranges and needn't reach their ends.
Inputs may be any that keep to these rules, and one draw needn't show every extreme that they name: The plan has 8 rounds: one round pairs every dp index with itself, and the others are the rounds of one round-robin plan of the 8 indices. The rows of partners hold each of these rounds once, in some order, so partners[r, partners[r, i]] = i.
All inputs are finite; a program needn't handle non-finite values.
Results may differ from the reference program's by a relative error of at most 0.02.
Values may be sent and summed in bfloat16 or wider, within the bound.
No kernel may reach another device: no remote copies, remote signals or barrier semaphores. Data moves between devices by JAX's collectives and lax.ppermute only.
A program may use at most 64 MiB of HBM per device.

```python
import math
import jax
import jax.numpy as jnp
from jax import lax

D = 4096
RANK = 64
LEN = 32
EX_DEV = 4
QRY_DEV = 2
SECTIONS = 16
ROUNDS = 8
TRAIN = 32
QUERIES = 16
TOKENS = 1024
N_SECTION = 16
N_DP = 8


def draw_partners(key, part):
    first_key, second_key = jax.random.split(jax.random.fold_in(key, 23), 2)
    picks = jax.random.permutation(first_key, N_DP).astype(jnp.int32)
    order = jax.random.permutation(second_key, N_DP).astype(jnp.int32)
    players = jnp.arange(N_DP, dtype=jnp.int32)
    row_list = []
    for round_at in range(ROUNDS):
        pick = picks[round_at]
        which = (pick - 1) % (N_DP - 1)
        other = (2 * which - players) % (N_DP - 1)
        mates = jnp.where(players == N_DP - 1, which, jnp.where(players == which, N_DP - 1, other))
        mates = jnp.where(pick == 0, players, mates)
        labelled = jnp.zeros((N_DP,), jnp.int32).at[order].set(order[mates])
        row_list.append(labelled)
    return jnp.stack(row_list).astype(jnp.int32)


def level_of(own_key, extent, pieces, smallest, high):
    loudness, own = 1.0, jax.random.fold_in(own_key, 6)
    for position, parts in pieces:
        draws = jnp.exp(jax.random.uniform(jax.random.fold_in(own, position), (parts,), jnp.float32, smallest / len(pieces), high / len(pieces)))
        loudness = loudness * jnp.repeat(draws, extent[position] // parts).reshape([-1 if axis == position else 1 for axis in range(len(extent))])
    return loudness


def bell_draw(key, extent, width, bound, shards=(), kind=jnp.bfloat16):
    loudness = level_of(key, extent, shards, -0.22, 0.18) if shards else 1.0
    values = jax.random.normal(key, extent, jnp.float32) * width * loudness
    return jnp.minimum(jnp.maximum(values, -bound), bound).astype(kind)


def setup_inputs(seed: int = 0) -> dict:
    arg_keys = jax.random.split(jax.random.key(seed), 9)
    return {
        "cotangent": bell_draw(arg_keys[0], (TOKENS, D), 1.0, 6.0, ((0, 8), (1, 4))),
        "saved_inputs": bell_draw(arg_keys[1], (SECTIONS, TOKENS, D), 1.0, 6.0, ((0, 16), (1, 8), (2, 4))),
        "pre_acts": bell_draw(arg_keys[2], (SECTIONS, TOKENS, D), 2.0, 8.0, ((0, 16), (1, 8), (2, 4))),
        "weights": bell_draw(arg_keys[3], (SECTIONS, D, D), (4 * D) ** -0.5, 0.046875, ((0, 16), (1, 4), (2, 8))),
        "proj_in": bell_draw(arg_keys[4], (SECTIONS, D, RANK), D ** -0.5, 0.09375, ((0, 16), (1, 4))),
        "proj_out": bell_draw(arg_keys[5], (SECTIONS, D, RANK), D ** -0.5, 0.09375, ((0, 16), (1, 4))),
        "query_panels": bell_draw(arg_keys[6], (SECTIONS, QUERIES, RANK * RANK), 0.5, 4.0, ((0, 16), (1, 8), (2, 4)), jnp.float32),
        "partners": draw_partners(jax.random.fold_in(arg_keys[8], 71), 0),
    }


def silu_slope(pre_state):
    sigma = jax.nn.sigmoid(pre_state)
    return sigma * (1.0 + pre_state * (1.0 - sigma))

def reference(cotangent, saved_inputs, pre_acts, weights, proj_in, proj_out, query_panels, partners):
    delta_grad = cotangent
    panel_list = []
    for layer in reversed(range(N_SECTION)):
        slopes = silu_slope(pre_acts[layer].astype(jnp.float32))
        unit_grad = (delta_grad.astype(jnp.float32) * slopes).astype(jnp.bfloat16)
        in_side = jnp.dot(saved_inputs[layer], proj_in[layer], preferred_element_type=jnp.float32)
        out_side = jnp.dot(unit_grad, proj_out[layer], preferred_element_type=jnp.float32)
        panel_here = jnp.einsum('etr,etc->erc', in_side.reshape(TRAIN, LEN, RANK), out_side.reshape(TRAIN, LEN, RANK), precision=lax.Precision.HIGHEST) / math.sqrt(LEN)
        panel_list.append(panel_here.reshape(TRAIN, RANK * RANK))
        back_term = jnp.dot(unit_grad, weights[layer].T, preferred_element_type=jnp.float32)
        delta_grad = (delta_grad.astype(jnp.float32) + back_term).astype(jnp.bfloat16)
    train_panels = jnp.stack(panel_list[::-1])
    query_view = query_panels.reshape(N_SECTION, N_DP, QRY_DEV, RANK * RANK)
    train_view = train_panels.reshape(N_SECTION, N_DP, EX_DEV, RANK * RANK)
    block_list = []
    for round_at in range(ROUNDS):
        chosen = jnp.take(train_view, partners[round_at].astype(jnp.int32), axis=1)
        block_list.append(jnp.einsum('sbqk,sbek->bqe', query_view, chosen, precision=lax.Precision.HIGHEST))
    stacked = jnp.stack(block_list, axis=1)
    scores = stacked.transpose(0, 2, 1, 3).reshape(QUERIES, ROUNDS, EX_DEV) / (RANK * math.sqrt(N_SECTION))
    return (train_panels, scores)
```

```python
import math

import jax
import jax.numpy as jnp
from jax import lax
from jax.sharding import PartitionSpec as P

LEN = 32
CHUNKS = 4


def silu_slope(pre_state):
    sigma = jax.nn.sigmoid(pre_state)
    return sigma * (1.0 + pre_state * (1.0 - sigma))


def to_every_width_piece_below(block, section_count, model_count, shift):
    route = [
        (s * model_count + m, (s - 1) * model_count + (m + shift) % model_count)
        for s in range(1, section_count)
        for m in range(model_count)
    ]
    return lax.ppermute(block, ("section", "mp"), route)


def body(cotangent, saved_inputs, pre_acts, weights, proj_in, proj_out, query_panels, partners):
    section_count = lax.axis_size("section")
    model_count = lax.axis_size("mp")
    data_count = lax.axis_size("dp")
    section_index = lax.axis_index("section")
    model_index = lax.axis_index("mp")
    data_index = lax.axis_index("dp")
    tokens = saved_inputs.shape[1]
    piece = saved_inputs.shape[2]
    width = piece * model_count
    length = LEN
    examples = tokens // length
    low_rank = proj_in.shape[2]
    chunk = tokens // CHUNKS
    chunk_examples = chunk // length
    top_section = section_count - 1
    piece_rank = low_rank // model_count

    w_rows = lax.all_gather(weights[0], "dp", axis=1, tiled=True)
    pre_full = lax.all_gather(pre_acts[0], "mp", axis=1, tiled=True)
    top_full = lax.all_gather(cotangent, "mp", axis=1, tiled=True)
    inputs_full = lax.all_gather(saved_inputs[0], "mp", axis=1, tiled=True)
    in_proj = lax.all_gather(proj_in[0], "mp", axis=0, tiled=True)
    out_proj = lax.all_gather(proj_out[0], "mp", axis=0, tiled=True)
    queries = lax.all_gather(query_panels[0], "dp", axis=0, tiled=True)
    slopes = silu_slope(pre_full.astype(jnp.float32))
    in_side = jnp.dot(inputs_full, in_proj, preferred_element_type=jnp.float32)
    in_rows = lax.dynamic_slice_in_dim(in_side, model_index * piece_rank, piece_rank, 1)

    panel_store = jnp.zeros((CHUNKS, chunk_examples, piece_rank * low_rank), jnp.float32)
    score_store = jnp.zeros((CHUNKS, queries.shape[0], chunk_examples), jnp.float32)
    outgoing = jnp.zeros((chunk, piece), jnp.bfloat16)
    is_top = section_index == top_section
    step_count = CHUNKS + section_count - 1
    for turn in range(step_count):
        if turn > 0:
            received = [
                to_every_width_piece_below(outgoing, section_count, model_count, shift)
                for shift in range(model_count)
            ]
            stacked = jnp.stack(received)
            order = (model_index - jnp.arange(model_count)) % model_count
            below_full = jnp.take(stacked, order, axis=0).transpose(1, 0, 2).reshape(chunk, width)
            below_mine = received[0]
        else:
            below_full = jnp.zeros((chunk, width), jnp.bfloat16)
            below_mine = jnp.zeros((chunk, piece), jnp.bfloat16)
        chunk_at = turn - (top_section - section_index)
        active = jnp.logical_and(chunk_at >= 0, chunk_at < CHUNKS)
        clipped = jnp.clip(chunk_at, 0, CHUNKS - 1)
        row_start = clipped * chunk
        top_rows = lax.dynamic_slice_in_dim(top_full, row_start, chunk, 0)
        delta_full = jnp.where(is_top, top_rows, below_full)
        top_mine = lax.dynamic_slice_in_dim(cotangent, row_start, chunk, 0)
        delta_mine = jnp.where(is_top, top_mine, below_mine)
        slope_rows = lax.dynamic_slice_in_dim(slopes, row_start, chunk, 0)
        grad = (delta_full.astype(jnp.float32) * slope_rows).astype(jnp.bfloat16)
        if turn < step_count - 1:
            back_term = lax.dot_general(
                grad, w_rows, (((1,), (1,)), ((), ())), preferred_element_type=jnp.float32
            )
            outgoing = (delta_mine.astype(jnp.float32) + back_term).astype(jnp.bfloat16)

        out_side = jnp.dot(grad, out_proj, preferred_element_type=jnp.float32)
        in_chunk = lax.dynamic_slice_in_dim(in_rows, row_start, chunk, 0)
        panels = jnp.einsum(
            "etr,etc->erc",
            in_chunk.reshape(chunk_examples, length, piece_rank),
            out_side.reshape(chunk_examples, length, low_rank),
            precision=lax.Precision.HIGHEST,
        ) / math.sqrt(length)
        panels = panels.reshape(chunk_examples, piece_rank * low_rank)
        partial = jnp.dot(queries, panels.T, precision=lax.Precision.HIGHEST)
        old_panels = lax.dynamic_index_in_dim(panel_store, clipped, 0, keepdims=False)
        panel_store = lax.dynamic_update_index_in_dim(
            panel_store, jnp.where(active, panels, old_panels), clipped, 0
        )
        old_scores = lax.dynamic_index_in_dim(score_store, clipped, 0, keepdims=False)
        score_store = lax.dynamic_update_index_in_dim(
            score_store, jnp.where(active, partial, old_scores), clipped, 0
        )

    panels_here = panel_store.reshape(examples, piece_rank * low_rank)
    asked = queries.shape[0]
    mine = score_store.transpose(1, 0, 2).reshape(asked, examples)
    table = jnp.zeros((asked, data_count * examples), jnp.float32)
    table = lax.dynamic_update_slice(table, mine, (jnp.int32(0), data_index * examples))
    score_scale = 1.0 / (low_rank * math.sqrt(section_count))
    summed = lax.psum(table * score_scale, ("section", "dp", "mp"))
    rounds = partners.shape[0]
    per_dp = asked // data_count
    owner = jnp.arange(asked) // per_dp
    chosen = partners[:, owner].T
    columns = chosen[:, :, None] * examples + jnp.arange(examples)[None, None, :]
    scores = jnp.take_along_axis(summed, columns.reshape(asked, rounds * examples), axis=1)
    scores = scores.reshape(asked, rounds, examples)
    return (panels_here[None], scores)


def solution(mesh):
    placed = (
        P("dp", "mp"),
        P("section", "dp", "mp"),
        P("section", "dp", "mp"),
        P("section", "mp", "dp"),
        P("section", "mp", None),
        P("section", "mp", None),
        P("section", "dp", "mp"),
        P(),
    )
    return jax.shard_map(
        body, mesh=mesh, in_specs=placed, out_specs=(P("section", "dp", "mp"), P()), check_vma=False
    )
```

```python
import math

import jax
import jax.numpy as jnp
from jax import lax
from jax.sharding import PartitionSpec as P

LEN = 32
CHUNKS = 2


def from_behind(block, axis, distance):
    devices = range(lax.axis_size(axis))
    route = [(i - distance, i) for i in devices if i - distance in devices]
    return lax.ppermute(block, axis, route)


def silu_slope(pre_state):
    sigma = jax.nn.sigmoid(pre_state)
    return sigma * (1.0 + pre_state * (1.0 - sigma))


def body(cotangent, saved_inputs, pre_acts, weights, proj_in, proj_out, query_panels, partners):
    section_count = lax.axis_size("section")
    model_count = lax.axis_size("mp")
    data_count = lax.axis_size("dp")
    section_index = lax.axis_index("section")
    model_index = lax.axis_index("mp")
    data_index = lax.axis_index("dp")
    tokens = saved_inputs.shape[1]
    piece = saved_inputs.shape[2]
    length = LEN
    examples = tokens // length
    low_rank = proj_in.shape[2]
    chunk = tokens // CHUNKS
    chunk_examples = chunk // length
    top_section = section_count - 1
    piece_rank = low_rank // model_count

    w_rows = lax.all_gather(weights[0], "dp", axis=1, tiled=True)
    slopes = silu_slope(pre_acts[0].astype(jnp.float32))
    out_proj = lax.all_gather(proj_out[0], "mp", axis=0, tiled=True)
    in_part = jnp.dot(saved_inputs[0], proj_in[0], preferred_element_type=jnp.float32)
    in_side = lax.psum(in_part, "mp")
    in_rows = lax.dynamic_slice_in_dim(in_side, model_index * piece_rank, piece_rank, 1)
    queries = query_panels[0]
    asked = queries.shape[0] * data_count
    queries = lax.all_gather(queries, "dp", axis=0, tiled=True)

    panel_store = jnp.zeros((CHUNKS, chunk_examples, piece_rank * low_rank), jnp.float32)
    score_store = jnp.zeros((CHUNKS, asked, chunk_examples), jnp.float32)
    outgoing = jnp.zeros((chunk, piece), jnp.bfloat16)
    is_top = section_index == top_section
    step_count = CHUNKS + section_count - 1
    for turn in range(step_count):
        chunk_at = turn - (top_section - section_index)
        active = jnp.logical_and(chunk_at >= 0, chunk_at < CHUNKS)
        clipped = jnp.clip(chunk_at, 0, CHUNKS - 1)
        row_start = clipped * chunk
        top_rows = lax.dynamic_slice_in_dim(cotangent, row_start, chunk, 0)
        if turn > 0:
            received = from_behind(outgoing, "section", -1)
            delta_piece = jnp.where(is_top, top_rows, received)
        else:
            delta_piece = top_rows
        slope_rows = lax.dynamic_slice_in_dim(slopes, row_start, chunk, 0)
        grad_piece = (delta_piece.astype(jnp.float32) * slope_rows).astype(jnp.bfloat16)
        grad_full = lax.all_gather(grad_piece, "mp", axis=1, tiled=True)
        if turn < step_count - 1:
            back_term = lax.dot_general(
                grad_full, w_rows, (((1,), (1,)), ((), ())), preferred_element_type=jnp.float32
            )
            outgoing = (delta_piece.astype(jnp.float32) + back_term).astype(jnp.bfloat16)

        out_side = jnp.dot(grad_full, out_proj, preferred_element_type=jnp.float32)
        in_chunk = lax.dynamic_slice_in_dim(in_rows, row_start, chunk, 0)
        panels = jnp.einsum(
            "etr,etc->erc",
            in_chunk.reshape(chunk_examples, length, piece_rank),
            out_side.reshape(chunk_examples, length, low_rank),
            precision=lax.Precision.HIGHEST,
        ) / math.sqrt(length)
        panels = panels.reshape(chunk_examples, piece_rank * low_rank)
        partial = jnp.dot(queries, panels.T, precision=lax.Precision.HIGHEST)
        old_panels = lax.dynamic_index_in_dim(panel_store, clipped, 0, keepdims=False)
        panel_store = lax.dynamic_update_index_in_dim(
            panel_store, jnp.where(active, panels, old_panels), clipped, 0
        )
        old_scores = lax.dynamic_index_in_dim(score_store, clipped, 0, keepdims=False)
        score_store = lax.dynamic_update_index_in_dim(
            score_store, jnp.where(active, partial, old_scores), clipped, 0
        )

    panels_here = panel_store.reshape(examples, piece_rank * low_rank)
    mine = score_store.transpose(1, 0, 2).reshape(asked, examples)
    table = jnp.zeros((asked, data_count * examples), jnp.float32)
    table = lax.dynamic_update_slice(table, mine, (jnp.int32(0), data_index * examples))
    score_scale = 1.0 / (low_rank * math.sqrt(section_count))
    summed = lax.psum(table * score_scale, "mp")
    summed = lax.psum(summed, "dp")
    summed = lax.psum(summed, "section")
    rounds = partners.shape[0]
    per_dp = asked // data_count
    owner = jnp.arange(asked) // per_dp
    chosen = partners[:, owner].T
    columns = chosen[:, :, None] * examples + jnp.arange(examples)[None, None, :]
    scores = jnp.take_along_axis(summed, columns.reshape(asked, rounds * examples), axis=1)
    scores = scores.reshape(asked, rounds, examples)
    return (panels_here[None], scores)


def solution(mesh):
    placed = (
        P("dp", "mp"),
        P("section", "dp", "mp"),
        P("section", "dp", "mp"),
        P("section", "mp", "dp"),
        P("section", "mp", None),
        P("section", "mp", None),
        P("section", "dp", "mp"),
        P(),
    )
    return jax.shard_map(
        body, mesh=mesh, in_specs=placed, out_specs=(P("section", "dp", "mp"), P()), check_vma=False
    )
```

```python
import math

import jax
import jax.numpy as jnp
from jax import lax
from jax.sharding import PartitionSpec as P

LEN = 32
CHUNKS = 2


def from_behind(block, axis, distance):
    devices = range(lax.axis_size(axis))
    route = [(i - distance, i) for i in devices if i - distance in devices]
    return lax.ppermute(block, axis, route)


def silu_slope(pre_state):
    sigma = jax.nn.sigmoid(pre_state)
    return sigma * (1.0 + pre_state * (1.0 - sigma))


def body(cotangent, saved_inputs, pre_acts, weights, proj_in, proj_out, query_panels, partners):
    section_count = lax.axis_size("section")
    model_count = lax.axis_size("mp")
    data_count = lax.axis_size("dp")
    section_index = lax.axis_index("section")
    model_index = lax.axis_index("mp")
    data_index = lax.axis_index("dp")
    tokens = saved_inputs.shape[1]
    piece = saved_inputs.shape[2]
    length = LEN
    examples = tokens // length
    low_rank = proj_in.shape[2]
    chunk = tokens // CHUNKS
    chunk_examples = chunk // length
    top_section = section_count - 1
    piece_rank = low_rank // model_count

    w_rows = lax.all_gather(weights[0], "dp", axis=1, tiled=True)
    slopes = silu_slope(pre_acts[0].astype(jnp.float32))
    out_proj = lax.all_gather(proj_out[0], "mp", axis=0, tiled=True)
    in_part = jnp.dot(saved_inputs[0], proj_in[0], preferred_element_type=jnp.float32)
    in_side = lax.psum(in_part, "mp")
    in_rows = lax.dynamic_slice_in_dim(in_side, model_index * piece_rank, piece_rank, 1)
    queries = query_panels[0]
    asked = queries.shape[0] * data_count
    queries = lax.all_gather(queries, "dp", axis=0, tiled=True)

    panel_store = jnp.zeros((CHUNKS, chunk_examples, piece_rank * low_rank), jnp.float32)
    score_store = jnp.zeros((CHUNKS, asked, chunk_examples), jnp.float32)
    outgoing = jnp.zeros((chunk, piece), jnp.bfloat16)
    is_top = section_index == top_section
    step_count = CHUNKS + section_count - 1
    for turn in range(step_count):
        chunk_at = turn - (top_section - section_index)
        active = jnp.logical_and(chunk_at >= 0, chunk_at < CHUNKS)
        clipped = jnp.clip(chunk_at, 0, CHUNKS - 1)
        row_start = clipped * chunk
        top_rows = lax.dynamic_slice_in_dim(cotangent, row_start, chunk, 0)
        if turn > 0:
            received = from_behind(outgoing, "section", -1)
            delta_piece = jnp.where(is_top, top_rows, received)
        else:
            delta_piece = top_rows
        slope_rows = lax.dynamic_slice_in_dim(slopes, row_start, chunk, 0)
        grad_piece = (delta_piece.astype(jnp.float32) * slope_rows).astype(jnp.bfloat16)
        grad_full = lax.all_gather(grad_piece, "mp", axis=1, tiled=True)
        if turn < step_count - 1:
            back_term = lax.dot_general(
                grad_full, w_rows, (((1,), (1,)), ((), ())), preferred_element_type=jnp.float32
            )
            outgoing = (delta_piece.astype(jnp.float32) + back_term).astype(jnp.bfloat16)

        out_side = jnp.dot(grad_full, out_proj, preferred_element_type=jnp.float32)
        in_chunk = lax.dynamic_slice_in_dim(in_rows, row_start, chunk, 0)
        panels = jnp.einsum(
            "etr,etc->erc",
            in_chunk.reshape(chunk_examples, length, piece_rank),
            out_side.reshape(chunk_examples, length, low_rank),
            precision=lax.Precision.HIGHEST,
        ) / math.sqrt(length)
        panels = panels.reshape(chunk_examples, piece_rank * low_rank)
        partial = jnp.dot(queries, panels.T, precision=lax.Precision.HIGHEST)
        old_panels = lax.dynamic_index_in_dim(panel_store, clipped, 0, keepdims=False)
        panel_store = lax.dynamic_update_index_in_dim(
            panel_store, jnp.where(active, panels, old_panels), clipped, 0
        )
        old_scores = lax.dynamic_index_in_dim(score_store, clipped, 0, keepdims=False)
        score_store = lax.dynamic_update_index_in_dim(
            score_store, jnp.where(active, partial, old_scores), clipped, 0
        )

    panels_here = panel_store.reshape(examples, piece_rank * low_rank)
    mine = score_store.transpose(1, 0, 2).reshape(asked, examples)
    table = jnp.zeros((asked, data_count * examples), jnp.float32)
    table = lax.dynamic_update_slice(table, mine, (jnp.int32(0), data_index * examples))
    score_scale = 1.0 / (low_rank * math.sqrt(section_count))
    summed = table * score_scale
    everyone = ("mp", "dp", "section")
    total = section_count * data_count * model_count
    for level in range(total.bit_length() - 1):
        route = [(i, i ^ (1 << level)) for i in range(total)]
        summed = summed + lax.ppermute(summed, everyone[::-1], route)
    rounds = partners.shape[0]
    per_dp = asked // data_count
    owner = jnp.arange(asked) // per_dp
    chosen = partners[:, owner].T
    columns = chosen[:, :, None] * examples + jnp.arange(examples)[None, None, :]
    scores = jnp.take_along_axis(summed, columns.reshape(asked, rounds * examples), axis=1)
    scores = scores.reshape(asked, rounds, examples)
    return (panels_here[None], scores)


def solution(mesh):
    placed = (
        P("dp", "mp"),
        P("section", "dp", "mp"),
        P("section", "dp", "mp"),
        P("section", "mp", "dp"),
        P("section", "mp", None),
        P("section", "mp", None),
        P("section", "dp", "mp"),
        P(),
    )
    return jax.shard_map(
        body, mesh=mesh, in_specs=placed, out_specs=(P("section", "dp", "mp"), P()), check_vma=False
    )
```

```python
import math

import jax
import jax.numpy as jnp
from jax import lax
from jax.experimental.layout import Layout, with_layout_constraint
from jax.sharding import PartitionSpec as P

LEN = 32
CHUNKS = 2


def from_behind(block, axis, distance):
    devices = range(lax.axis_size(axis))
    route = [(i - distance, i) for i in devices if i - distance in devices]
    return lax.ppermute(block, axis, route)


def silu_slope(pre_state):
    sigma = jax.nn.sigmoid(pre_state)
    return sigma * (1.0 + pre_state * (1.0 - sigma))


def body(cotangent, saved_inputs, pre_acts, weights, proj_in, proj_out, query_panels, partners):
    section_count = lax.axis_size("section")
    model_count = lax.axis_size("mp")
    data_count = lax.axis_size("dp")
    section_index = lax.axis_index("section")
    model_index = lax.axis_index("mp")
    data_index = lax.axis_index("dp")
    tokens = saved_inputs.shape[1]
    piece = saved_inputs.shape[2]
    length = LEN
    examples = tokens // length
    low_rank = proj_in.shape[2]
    chunk = tokens // CHUNKS
    chunk_examples = chunk // length
    top_section = section_count - 1
    piece_rank = low_rank // model_count

    w_cols = lax.all_gather(weights[0].T, "dp", axis=0, tiled=True)
    w_cols = with_layout_constraint(w_cols, Layout(major_to_minor=(0, 1)))
    slopes = silu_slope(pre_acts[0].astype(jnp.float32))
    out_proj = lax.all_gather(proj_out[0], "mp", axis=0, tiled=True)
    in_part = jnp.dot(saved_inputs[0], proj_in[0], preferred_element_type=jnp.float32)
    in_side = lax.psum(in_part, "mp")
    in_rows = lax.dynamic_slice_in_dim(in_side, model_index * piece_rank, piece_rank, 1)
    queries = query_panels[0]
    asked = queries.shape[0] * data_count
    queries = lax.all_gather(queries, "dp", axis=0, tiled=True)

    panel_store = jnp.zeros((CHUNKS, chunk_examples, piece_rank * low_rank), jnp.float32)
    score_store = jnp.zeros((CHUNKS, asked, chunk_examples), jnp.float32)
    outgoing = jnp.zeros((chunk, piece), jnp.bfloat16)
    is_top = section_index == top_section
    step_count = CHUNKS + section_count - 1
    for turn in range(step_count):
        chunk_at = turn - (top_section - section_index)
        active = jnp.logical_and(chunk_at >= 0, chunk_at < CHUNKS)
        clipped = jnp.clip(chunk_at, 0, CHUNKS - 1)
        row_start = clipped * chunk
        top_rows = lax.dynamic_slice_in_dim(cotangent, row_start, chunk, 0)
        if turn > 0:
            received = from_behind(outgoing, "section", -1)
            delta_piece = jnp.where(is_top, top_rows, received)
        else:
            delta_piece = top_rows
        slope_rows = lax.dynamic_slice_in_dim(slopes, row_start, chunk, 0)
        grad_piece = (delta_piece.astype(jnp.float32) * slope_rows).astype(jnp.bfloat16)
        grad_full = lax.all_gather(grad_piece, "mp", axis=1, tiled=True)
        if turn < step_count - 1:
            back_term = jnp.dot(grad_full, w_cols, preferred_element_type=jnp.float32)
            outgoing = (delta_piece.astype(jnp.float32) + back_term).astype(jnp.bfloat16)

        out_side = jnp.dot(grad_full, out_proj, preferred_element_type=jnp.float32)
        in_chunk = lax.dynamic_slice_in_dim(in_rows, row_start, chunk, 0)
        panels = jnp.einsum(
            "etr,etc->erc",
            in_chunk.reshape(chunk_examples, length, piece_rank),
            out_side.reshape(chunk_examples, length, low_rank),
            precision=lax.Precision.HIGHEST,
        ) / math.sqrt(length)
        panels = panels.reshape(chunk_examples, piece_rank * low_rank)
        partial = jnp.dot(queries, panels.T, precision=lax.Precision.HIGHEST)
        old_panels = lax.dynamic_index_in_dim(panel_store, clipped, 0, keepdims=False)
        panel_store = lax.dynamic_update_index_in_dim(
            panel_store, jnp.where(active, panels, old_panels), clipped, 0
        )
        old_scores = lax.dynamic_index_in_dim(score_store, clipped, 0, keepdims=False)
        score_store = lax.dynamic_update_index_in_dim(
            score_store, jnp.where(active, partial, old_scores), clipped, 0
        )

    panels_here = panel_store.reshape(examples, piece_rank * low_rank)
    mine = score_store.transpose(1, 0, 2).reshape(asked, examples)
    table = jnp.zeros((asked, data_count * examples), jnp.float32)
    table = lax.dynamic_update_slice(table, mine, (jnp.int32(0), data_index * examples))
    score_scale = 1.0 / (low_rank * math.sqrt(section_count))
    summed = table * score_scale
    everyone = ("mp", "dp", "section")
    total = section_count * data_count * model_count
    for level in range(total.bit_length() - 1):
        route = [(i, i ^ (1 << level)) for i in range(total)]
        summed = summed + lax.ppermute(summed, everyone[::-1], route)
    rounds = partners.shape[0]
    per_dp = asked // data_count
    owner = jnp.arange(asked) // per_dp
    chosen = partners[:, owner].T
    columns = chosen[:, :, None] * examples + jnp.arange(examples)[None, None, :]
    scores = jnp.take_along_axis(summed, columns.reshape(asked, rounds * examples), axis=1)
    scores = scores.reshape(asked, rounds, examples)
    return (panels_here[None], scores)


def solution(mesh):
    placed = (
        P("dp", "mp"),
        P("section", "dp", "mp"),
        P("section", "dp", "mp"),
        P("section", "mp", "dp"),
        P("section", "mp", None),
        P("section", "mp", None),
        P("section", "dp", "mp"),
        P(),
    )
    return jax.shard_map(
        body, mesh=mesh, in_specs=placed, out_specs=(P("section", "dp", "mp"), P()), check_vma=False
    )
```

```python
import math

import jax
import jax.numpy as jnp
from jax import lax
from jax.experimental.layout import Layout, with_layout_constraint
from jax.sharding import PartitionSpec as P

LEN = 32
CHUNKS = 2


def from_behind(block, axis, distance):
    devices = range(lax.axis_size(axis))
    route = [(i - distance, i) for i in devices if i - distance in devices]
    return lax.ppermute(block, axis, route)


def silu_slope(pre_state):
    sigma = jax.nn.sigmoid(pre_state)
    return sigma * (1.0 + pre_state * (1.0 - sigma))


def body(cotangent, saved_inputs, pre_acts, weights, proj_in, proj_out, query_panels, partners):
    section_count = lax.axis_size("section")
    model_count = lax.axis_size("mp")
    data_count = lax.axis_size("dp")
    section_index = lax.axis_index("section")
    model_index = lax.axis_index("mp")
    data_index = lax.axis_index("dp")
    tokens = saved_inputs.shape[1]
    piece = saved_inputs.shape[2]
    length = LEN
    examples = tokens // length
    low_rank = proj_in.shape[2]
    chunk = tokens // CHUNKS
    chunk_examples = chunk // length
    top_section = section_count - 1
    piece_rank = low_rank // model_count

    w_cols = lax.all_gather(weights[0].T, "dp", axis=0, tiled=True)
    w_cols = with_layout_constraint(w_cols, Layout(major_to_minor=(0, 1)))
    slopes = silu_slope(pre_acts[0].astype(jnp.float32))
    out_proj = lax.all_gather(proj_out[0], "mp", axis=0, tiled=True)
    in_part = jnp.dot(saved_inputs[0], proj_in[0], preferred_element_type=jnp.float32)
    in_side = lax.psum(in_part, "mp")
    queries = lax.all_gather(query_panels[0], "mp", axis=1, tiled=True)
    asked = queries.shape[0] * data_count
    queries = lax.all_gather(queries, "dp", axis=0, tiled=True)

    panel_store = jnp.zeros((CHUNKS, chunk_examples, piece_rank * low_rank), jnp.float32)
    score_store = jnp.zeros((CHUNKS, asked, chunk_examples), jnp.float32)
    outgoing = jnp.zeros((chunk, piece), jnp.bfloat16)
    is_top = section_index == top_section
    step_count = CHUNKS + section_count - 1
    for turn in range(step_count):
        chunk_at = turn - (top_section - section_index)
        active = jnp.logical_and(chunk_at >= 0, chunk_at < CHUNKS)
        clipped = jnp.clip(chunk_at, 0, CHUNKS - 1)
        row_start = clipped * chunk
        top_rows = lax.dynamic_slice_in_dim(cotangent, row_start, chunk, 0)
        if turn > 0:
            received = from_behind(outgoing, "section", -1)
            delta_piece = jnp.where(is_top, top_rows, received)
        else:
            delta_piece = top_rows
        slope_rows = lax.dynamic_slice_in_dim(slopes, row_start, chunk, 0)
        grad_piece = (delta_piece.astype(jnp.float32) * slope_rows).astype(jnp.bfloat16)
        grad_full = lax.all_gather(grad_piece, "mp", axis=1, tiled=True)
        if turn < step_count - 1:
            back_term = jnp.dot(grad_full, w_cols, preferred_element_type=jnp.float32)
            outgoing = (delta_piece.astype(jnp.float32) + back_term).astype(jnp.bfloat16)

        out_side = jnp.dot(grad_full, out_proj, preferred_element_type=jnp.float32)
        in_chunk = lax.dynamic_slice_in_dim(in_side, row_start, chunk, 0)
        whole = jnp.einsum(
            "etr,etc->erc",
            in_chunk.reshape(chunk_examples, length, low_rank),
            out_side.reshape(chunk_examples, length, low_rank),
            precision=lax.Precision.HIGHEST,
        ) / math.sqrt(length)
        partial = jnp.dot(
            queries, whole.reshape(chunk_examples, low_rank * low_rank).T, precision=lax.Precision.HIGHEST
        )
        panels = lax.dynamic_slice_in_dim(whole, model_index * piece_rank, piece_rank, 1)
        panels = panels.reshape(chunk_examples, piece_rank * low_rank)
        old_panels = lax.dynamic_index_in_dim(panel_store, clipped, 0, keepdims=False)
        panel_store = lax.dynamic_update_index_in_dim(
            panel_store, jnp.where(active, panels, old_panels), clipped, 0
        )
        old_scores = lax.dynamic_index_in_dim(score_store, clipped, 0, keepdims=False)
        score_store = lax.dynamic_update_index_in_dim(
            score_store, jnp.where(active, partial, old_scores), clipped, 0
        )

    panels_here = panel_store.reshape(examples, piece_rank * low_rank)
    mine = score_store.transpose(1, 0, 2).reshape(asked, examples)
    score_scale = 1.0 / (low_rank * math.sqrt(section_count))
    per_dp = asked // data_count
    owner = jnp.arange(asked) // per_dp
    meets = partners[:, owner].T == data_index
    scores = jnp.where(meets[:, :, None], mine[:, None, :] * score_scale, 0.0)
    everyone = ("dp", "section")
    total = section_count * data_count
    for level in range(total.bit_length() - 1):
        route = [(i, i ^ (1 << level)) for i in range(total)]
        scores = scores + lax.ppermute(scores, everyone[::-1], route)
    return (panels_here[None], scores)


def solution(mesh):
    placed = (
        P("dp", "mp"),
        P("section", "dp", "mp"),
        P("section", "dp", "mp"),
        P("section", "mp", "dp"),
        P("section", "mp", None),
        P("section", "mp", None),
        P("section", "dp", "mp"),
        P(),
    )
    return jax.shard_map(
        body, mesh=mesh, in_specs=placed, out_specs=(P("section", "dp", "mp"), P()), check_vma=False
    )
```

```python
import math

import jax
import jax.numpy as jnp
from jax import lax
from jax.experimental.layout import Layout, with_layout_constraint
from jax.sharding import PartitionSpec as P

LEN = 32
CHUNKS = 2


def silu_slope(pre_state):
    sigma = jax.nn.sigmoid(pre_state)
    return sigma * (1.0 + pre_state * (1.0 - sigma))


def body(cotangent, saved_inputs, pre_acts, weights, proj_in, proj_out, query_panels, partners):
    section_count = lax.axis_size("section")
    model_count = lax.axis_size("mp")
    data_count = lax.axis_size("dp")
    section_index = lax.axis_index("section")
    model_index = lax.axis_index("mp")
    data_index = lax.axis_index("dp")
    tokens = saved_inputs.shape[1]
    piece = saved_inputs.shape[2]
    length = LEN
    examples = tokens // length
    low_rank = proj_in.shape[2]
    chunk = tokens // CHUNKS
    chunk_examples = chunk // length
    top_section = section_count - 1
    piece_rank = low_rank // model_count

    w_cols = lax.all_gather(weights[0].T, "dp", axis=0, tiled=True)
    w_cols = with_layout_constraint(w_cols, Layout(major_to_minor=(0, 1)))
    slopes = silu_slope(pre_acts[0].astype(jnp.float32))
    out_proj = lax.all_gather(proj_out[0], "mp", axis=0, tiled=True)
    in_part = jnp.dot(saved_inputs[0], proj_in[0], preferred_element_type=jnp.float32)
    in_side = lax.psum(in_part, "mp")
    queries = lax.all_gather(query_panels[0], "mp", axis=1, tiled=True)
    asked = queries.shape[0] * data_count
    queries = lax.all_gather(queries, "dp", axis=0, tiled=True)

    panel_store = jnp.zeros((CHUNKS, chunk_examples, piece_rank * low_rank), jnp.float32)
    score_store = jnp.zeros((CHUNKS, asked, chunk_examples), jnp.float32)
    outgoing = jnp.zeros((chunk, piece), jnp.bfloat16)
    is_top = section_index == top_section
    step_count = CHUNKS + section_count - 1
    for turn in range(step_count):
        chunk_at = turn - (top_section - section_index)
        active = jnp.logical_and(chunk_at >= 0, chunk_at < CHUNKS)
        clipped = jnp.clip(chunk_at, 0, CHUNKS - 1)
        row_start = clipped * chunk
        top_rows = lax.dynamic_slice_in_dim(cotangent, row_start, chunk, 0)
        if turn > 0:
            senders = [
                k for k in range(top_section + 1 - turn, top_section + 1 - turn + CHUNKS)
                if 1 <= k <= top_section
            ]
            received = lax.ppermute(outgoing, "section", [(k, k - 1) for k in senders])
            delta_piece = jnp.where(is_top, top_rows, received)
        else:
            delta_piece = top_rows
        slope_rows = lax.dynamic_slice_in_dim(slopes, row_start, chunk, 0)
        grad_piece = (delta_piece.astype(jnp.float32) * slope_rows).astype(jnp.bfloat16)
        grad_full = lax.all_gather(grad_piece, "mp", axis=1, tiled=True)
        if turn < step_count - 1:
            back_term = jnp.dot(grad_full, w_cols, preferred_element_type=jnp.float32)
            outgoing = (delta_piece.astype(jnp.float32) + back_term).astype(jnp.bfloat16)

        out_side = jnp.dot(grad_full, out_proj, preferred_element_type=jnp.float32)
        in_chunk = lax.dynamic_slice_in_dim(in_side, row_start, chunk, 0)
        whole = jnp.einsum(
            "etr,etc->erc",
            in_chunk.reshape(chunk_examples, length, low_rank),
            out_side.reshape(chunk_examples, length, low_rank),
            precision=lax.Precision.HIGHEST,
        ) / math.sqrt(length)
        partial = jnp.dot(
            queries, whole.reshape(chunk_examples, low_rank * low_rank).T, precision=lax.Precision.HIGHEST
        )
        panels = lax.dynamic_slice_in_dim(whole, model_index * piece_rank, piece_rank, 1)
        panels = panels.reshape(chunk_examples, piece_rank * low_rank)
        old_panels = lax.dynamic_index_in_dim(panel_store, clipped, 0, keepdims=False)
        panel_store = lax.dynamic_update_index_in_dim(
            panel_store, jnp.where(active, panels, old_panels), clipped, 0
        )
        old_scores = lax.dynamic_index_in_dim(score_store, clipped, 0, keepdims=False)
        score_store = lax.dynamic_update_index_in_dim(
            score_store, jnp.where(active, partial, old_scores), clipped, 0
        )

    panels_here = panel_store.reshape(examples, piece_rank * low_rank)
    mine = score_store.transpose(1, 0, 2).reshape(asked, examples)
    score_scale = 1.0 / (low_rank * math.sqrt(section_count))
    per_dp = asked // data_count
    owner = jnp.arange(asked) // per_dp
    meets = partners[:, owner].T == data_index
    scores = jnp.where(meets[:, :, None], mine[:, None, :] * score_scale, 0.0)
    total = section_count * data_count
    levels = list(range(total.bit_length() - 1))
    dp_levels = data_count.bit_length() - 1
    for level in levels[dp_levels:] + levels[:dp_levels]:
        route = [(i, i ^ (1 << level)) for i in range(total)]
        scores = scores + lax.ppermute(scores, ("section", "dp"), route)
    return (panels_here[None], scores)


def solution(mesh):
    placed = (
        P("dp", "mp"),
        P("section", "dp", "mp"),
        P("section", "dp", "mp"),
        P("section", "mp", "dp"),
        P("section", "mp", None),
        P("section", "mp", None),
        P("section", "dp", "mp"),
        P(),
    )
    return jax.shard_map(
        body, mesh=mesh, in_specs=placed, out_specs=(P("section", "dp", "mp"), P()), check_vma=False
    )
```

```python
import math

import jax
import jax.numpy as jnp
from jax import lax
from jax.experimental.layout import Layout, with_layout_constraint
from jax.sharding import PartitionSpec as P

LEN = 32
CHUNKS = 2


def silu_slope(pre_state):
    sigma = jax.nn.sigmoid(pre_state)
    return sigma * (1.0 + pre_state * (1.0 - sigma))


def group_sum(block, place, total, stride, ways):
    sent = [block]
    for shift in range(1, ways):
        route = []
        for i in range(total):
            here = (i // stride) % ways
            route.append((i, i + (((here + shift) % ways) - here) * stride))
        sent.append(lax.ppermute(block, ("section", "dp"), route))
    here = (place // stride) % ways
    ordered = jnp.take(jnp.stack(sent), (here - jnp.arange(ways)) % ways, axis=0)
    summed = ordered[0]
    for position in range(1, ways):
        summed = summed + ordered[position]
    return summed


def body(cotangent, saved_inputs, pre_acts, weights, proj_in, proj_out, query_panels, partners):
    section_count = lax.axis_size("section")
    model_count = lax.axis_size("mp")
    data_count = lax.axis_size("dp")
    section_index = lax.axis_index("section")
    model_index = lax.axis_index("mp")
    data_index = lax.axis_index("dp")
    tokens = saved_inputs.shape[1]
    piece = saved_inputs.shape[2]
    length = LEN
    examples = tokens // length
    low_rank = proj_in.shape[2]
    chunk = tokens // CHUNKS
    chunk_examples = chunk // length
    top_section = section_count - 1
    piece_rank = low_rank // model_count

    w_cols = lax.all_gather(weights[0].T, "dp", axis=0, tiled=True)
    w_cols = with_layout_constraint(w_cols, Layout(major_to_minor=(0, 1)))
    slopes = silu_slope(pre_acts[0].astype(jnp.float32))
    out_proj = lax.all_gather(proj_out[0], "mp", axis=0, tiled=True)
    in_part = jnp.dot(saved_inputs[0], proj_in[0], preferred_element_type=jnp.float32)
    in_side = lax.psum(in_part, "mp")
    queries = lax.all_gather(query_panels[0], "mp", axis=1, tiled=True)
    asked = queries.shape[0] * data_count
    queries = lax.all_gather(queries, "dp", axis=0, tiled=True)

    panel_store = jnp.zeros((CHUNKS, chunk_examples, piece_rank * low_rank), jnp.float32)
    score_store = jnp.zeros((CHUNKS, asked, chunk_examples), jnp.float32)
    outgoing = jnp.zeros((chunk, piece), jnp.bfloat16)
    is_top = section_index == top_section
    step_count = CHUNKS + section_count - 1
    for turn in range(step_count):
        chunk_at = turn - (top_section - section_index)
        active = jnp.logical_and(chunk_at >= 0, chunk_at < CHUNKS)
        clipped = jnp.clip(chunk_at, 0, CHUNKS - 1)
        row_start = clipped * chunk
        top_rows = lax.dynamic_slice_in_dim(cotangent, row_start, chunk, 0)
        if turn > 0:
            senders = [
                k for k in range(top_section + 1 - turn, top_section + 1 - turn + CHUNKS)
                if 1 <= k <= top_section
            ]
            received = lax.ppermute(outgoing, "section", [(k, k - 1) for k in senders])
            delta_piece = jnp.where(is_top, top_rows, received)
        else:
            delta_piece = top_rows
        slope_rows = lax.dynamic_slice_in_dim(slopes, row_start, chunk, 0)
        grad_piece = (delta_piece.astype(jnp.float32) * slope_rows).astype(jnp.bfloat16)
        grad_full = lax.all_gather(grad_piece, "mp", axis=1, tiled=True)
        if turn < step_count - 1:
            back_term = jnp.dot(grad_full, w_cols, preferred_element_type=jnp.float32)
            outgoing = (delta_piece.astype(jnp.float32) + back_term).astype(jnp.bfloat16)

        out_side = jnp.dot(grad_full, out_proj, preferred_element_type=jnp.float32)
        in_chunk = lax.dynamic_slice_in_dim(in_side, row_start, chunk, 0)
        whole = jnp.einsum(
            "etr,etc->erc",
            in_chunk.reshape(chunk_examples, length, low_rank),
            out_side.reshape(chunk_examples, length, low_rank),
            precision=lax.Precision.HIGHEST,
        ) / math.sqrt(length)
        partial = jnp.dot(
            queries, whole.reshape(chunk_examples, low_rank * low_rank).T, precision=lax.Precision.HIGHEST
        )
        panels = lax.dynamic_slice_in_dim(whole, model_index * piece_rank, piece_rank, 1)
        panels = panels.reshape(chunk_examples, piece_rank * low_rank)
        old_panels = lax.dynamic_index_in_dim(panel_store, clipped, 0, keepdims=False)
        panel_store = lax.dynamic_update_index_in_dim(
            panel_store, jnp.where(active, panels, old_panels), clipped, 0
        )
        old_scores = lax.dynamic_index_in_dim(score_store, clipped, 0, keepdims=False)
        score_store = lax.dynamic_update_index_in_dim(
            score_store, jnp.where(active, partial, old_scores), clipped, 0
        )

    panels_here = panel_store.reshape(examples, piece_rank * low_rank)
    mine = score_store.transpose(1, 0, 2).reshape(asked, examples)
    score_scale = 1.0 / (low_rank * math.sqrt(section_count))
    per_dp = asked // data_count
    owner = jnp.arange(asked) // per_dp
    meets = partners[:, owner].T == data_index
    scores = jnp.where(meets[:, :, None], mine[:, None, :] * score_scale, 0.0)
    place = section_index * data_count + data_index
    total = section_count * data_count
    stride = 1
    for ways in (4, 2) if data_count == 8 else (data_count,):
        scores = group_sum(scores, place, total, stride, ways)
        stride *= ways
    left = section_count
    while left > 1:
        ways = 4 if left % 4 == 0 else 2
        scores = group_sum(scores, place, total, stride, ways)
        stride *= ways
        left //= ways
    return (panels_here[None], scores)


def solution(mesh):
    placed = (
        P("dp", "mp"),
        P("section", "dp", "mp"),
        P("section", "dp", "mp"),
        P("section", "mp", "dp"),
        P("section", "mp", None),
        P("section", "mp", None),
        P("section", "dp", "mp"),
        P(),
    )
    return jax.shard_map(
        body, mesh=mesh, in_specs=placed, out_specs=(P("section", "dp", "mp"), P()), check_vma=False
    )
```

```python
import math

import jax
import jax.numpy as jnp
from jax import lax
from jax.experimental.layout import Layout, with_layout_constraint
from jax.sharding import PartitionSpec as P

LEN = 32
CHUNKS = 4


def silu_slope(pre_state):
    sigma = jax.nn.sigmoid(pre_state)
    return sigma * (1.0 + pre_state * (1.0 - sigma))


def body(cotangent, saved_inputs, pre_acts, weights, proj_in, proj_out, query_panels, partners):
    section_count = lax.axis_size("section")
    model_count = lax.axis_size("mp")
    data_count = lax.axis_size("dp")
    section_index = lax.axis_index("section")
    model_index = lax.axis_index("mp")
    data_index = lax.axis_index("dp")
    tokens = saved_inputs.shape[1]
    piece = saved_inputs.shape[2]
    length = LEN
    examples = tokens // length
    low_rank = proj_in.shape[2]
    chunk = tokens // CHUNKS
    chunk_examples = chunk // length
    top_section = section_count - 1
    piece_rank = low_rank // model_count

    w_cols = lax.all_gather(weights[0].T, "dp", axis=0, tiled=True)
    w_cols = with_layout_constraint(w_cols, Layout(major_to_minor=(0, 1)))
    slopes = silu_slope(pre_acts[0].astype(jnp.float32))
    out_proj = lax.all_gather(proj_out[0], "mp", axis=0, tiled=True)
    in_part = jnp.dot(saved_inputs[0], proj_in[0], preferred_element_type=jnp.float32)
    in_side = lax.psum(in_part, "mp")
    queries = lax.all_gather(query_panels[0], "mp", axis=1, tiled=True)
    asked = queries.shape[0] * data_count
    queries = lax.all_gather(queries, "dp", axis=0, tiled=True)

    panel_store = jnp.zeros((CHUNKS, chunk_examples, piece_rank * low_rank), jnp.float32)
    score_store = jnp.zeros((CHUNKS, asked, chunk_examples), jnp.float32)
    outgoing = jnp.zeros((chunk, piece), jnp.bfloat16)
    is_top = section_index == top_section
    step_count = CHUNKS + section_count - 1
    for turn in range(step_count):
        chunk_at = turn - (top_section - section_index)
        active = jnp.logical_and(chunk_at >= 0, chunk_at < CHUNKS)
        clipped = jnp.clip(chunk_at, 0, CHUNKS - 1)
        row_start = clipped * chunk
        top_rows = lax.dynamic_slice_in_dim(cotangent, row_start, chunk, 0)
        if turn > 0:
            senders = [
                k for k in range(top_section + 1 - turn, top_section + 1 - turn + CHUNKS)
                if 1 <= k <= top_section
            ]
            received = lax.ppermute(outgoing, "section", [(k, k - 1) for k in senders])
            delta_piece = jnp.where(is_top, top_rows, received)
        else:
            delta_piece = top_rows
        slope_rows = lax.dynamic_slice_in_dim(slopes, row_start, chunk, 0)
        grad_piece = (delta_piece.astype(jnp.float32) * slope_rows).astype(jnp.bfloat16)
        grad_full = lax.all_gather(grad_piece, "mp", axis=1, tiled=True)
        if turn < step_count - 1:
            back_term = jnp.dot(grad_full, w_cols, preferred_element_type=jnp.float32)
            outgoing = (delta_piece.astype(jnp.float32) + back_term).astype(jnp.bfloat16)

        out_side = jnp.dot(grad_full, out_proj, preferred_element_type=jnp.float32)
        in_chunk = lax.dynamic_slice_in_dim(in_side, row_start, chunk, 0)
        whole = jnp.einsum(
            "etr,etc->erc",
            in_chunk.reshape(chunk_examples, length, low_rank),
            out_side.reshape(chunk_examples, length, low_rank),
            precision=lax.Precision.HIGHEST,
        ) / math.sqrt(length)
        partial = jnp.dot(
            queries, whole.reshape(chunk_examples, low_rank * low_rank).T, precision=lax.Precision.HIGHEST
        )
        panels = lax.dynamic_slice_in_dim(whole, model_index * piece_rank, piece_rank, 1)
        panels = panels.reshape(chunk_examples, piece_rank * low_rank)
        old_panels = lax.dynamic_index_in_dim(panel_store, clipped, 0, keepdims=False)
        panel_store = lax.dynamic_update_index_in_dim(
            panel_store, jnp.where(active, panels, old_panels), clipped, 0
        )
        old_scores = lax.dynamic_index_in_dim(score_store, clipped, 0, keepdims=False)
        score_store = lax.dynamic_update_index_in_dim(
            score_store, jnp.where(active, partial, old_scores), clipped, 0
        )

    panels_here = panel_store.reshape(examples, piece_rank * low_rank)
    mine = score_store.transpose(1, 0, 2).reshape(asked, examples)
    score_scale = 1.0 / (low_rank * math.sqrt(section_count))
    per_dp = asked // data_count
    owner = jnp.arange(asked) // per_dp
    meets = partners[:, owner].T == data_index
    scores = jnp.where(meets[:, :, None], mine[:, None, :] * score_scale, 0.0)
    total = section_count * data_count
    levels = list(range(total.bit_length() - 1))
    dp_levels = data_count.bit_length() - 1
    for level in levels[dp_levels:] + levels[:dp_levels]:
        route = [(i, i ^ (1 << level)) for i in range(total)]
        scores = scores + lax.ppermute(scores, ("section", "dp"), route)
    return (panels_here[None], scores)


def solution(mesh):
    placed = (
        P("dp", "mp"),
        P("section", "dp", "mp"),
        P("section", "dp", "mp"),
        P("section", "mp", "dp"),
        P("section", "mp", None),
        P("section", "mp", None),
        P("section", "dp", "mp"),
        P(),
    )
    return jax.shard_map(
        body, mesh=mesh, in_specs=placed, out_specs=(P("section", "dp", "mp"), P()), check_vma=False
    )
```

```python
import math

import jax
import jax.numpy as jnp
from jax import lax
from jax.experimental.layout import Layout, with_layout_constraint
from jax.sharding import PartitionSpec as P

LEN = 32
CHUNKS = 2


def silu_slope(pre_state):
    sigma = jax.nn.sigmoid(pre_state)
    return sigma * (1.0 + pre_state * (1.0 - sigma))


def body(cotangent, saved_inputs, pre_acts, weights, proj_in, proj_out, query_panels, partners):
    section_count = lax.axis_size("section")
    model_count = lax.axis_size("mp")
    data_count = lax.axis_size("dp")
    section_index = lax.axis_index("section")
    model_index = lax.axis_index("mp")
    data_index = lax.axis_index("dp")
    tokens = saved_inputs.shape[1]
    piece = saved_inputs.shape[2]
    length = LEN
    examples = tokens // length
    low_rank = proj_in.shape[2]
    chunk = tokens // CHUNKS
    chunk_examples = chunk // length
    top_section = section_count - 1
    piece_rank = low_rank // model_count

    w_cols = lax.all_gather(weights[0].T, "dp", axis=0, tiled=True)
    w_cols = with_layout_constraint(w_cols, Layout(major_to_minor=(0, 1)))
    slopes = silu_slope(pre_acts[0].astype(jnp.float32))
    out_proj = lax.all_gather(proj_out[0], "mp", axis=0, tiled=True)
    in_part = jnp.dot(saved_inputs[0], proj_in[0], preferred_element_type=jnp.float32)
    in_side = lax.psum(in_part, "mp")
    queries = lax.all_gather(query_panels[0], "mp", axis=1, tiled=True)
    asked = queries.shape[0] * data_count
    queries = lax.all_gather(queries, "dp", axis=0, tiled=True)

    grad_store = jnp.zeros((CHUNKS, chunk, piece * model_count), jnp.bfloat16)
    outgoing = jnp.zeros((chunk, piece), jnp.bfloat16)
    is_top = section_index == top_section
    step_count = CHUNKS + section_count - 1
    for turn in range(step_count):
        chunk_at = turn - (top_section - section_index)
        active = jnp.logical_and(chunk_at >= 0, chunk_at < CHUNKS)
        clipped = jnp.clip(chunk_at, 0, CHUNKS - 1)
        row_start = clipped * chunk
        top_rows = lax.dynamic_slice_in_dim(cotangent, row_start, chunk, 0)
        if turn > 0:
            senders = [
                k for k in range(top_section + 1 - turn, top_section + 1 - turn + CHUNKS)
                if 1 <= k <= top_section
            ]
            received = lax.ppermute(outgoing, "section", [(k, k - 1) for k in senders])
            delta_piece = jnp.where(is_top, top_rows, received)
        else:
            delta_piece = top_rows
        slope_rows = lax.dynamic_slice_in_dim(slopes, row_start, chunk, 0)
        grad_piece = (delta_piece.astype(jnp.float32) * slope_rows).astype(jnp.bfloat16)
        grad_full = lax.all_gather(grad_piece, "mp", axis=1, tiled=True)
        if turn < step_count - 1:
            back_term = jnp.dot(grad_full, w_cols, preferred_element_type=jnp.float32)
            outgoing = (delta_piece.astype(jnp.float32) + back_term).astype(jnp.bfloat16)

        previous = lax.dynamic_index_in_dim(grad_store, clipped, 0, keepdims=False)
        grad_store = lax.dynamic_update_index_in_dim(
            grad_store, jnp.where(active, grad_full, previous), clipped, 0
        )

    grads = grad_store.reshape(tokens, piece * model_count)
    out_side = jnp.dot(grads, out_proj, preferred_element_type=jnp.float32)
    whole = jnp.einsum(
        "etr,etc->erc",
        in_side.reshape(examples, length, low_rank),
        out_side.reshape(examples, length, low_rank),
        precision=lax.Precision.HIGHEST,
    ) / math.sqrt(length)
    mine = jnp.dot(
        queries, whole.reshape(examples, low_rank * low_rank).T, precision=lax.Precision.HIGHEST
    )
    panels_here = lax.dynamic_slice_in_dim(whole, model_index * piece_rank, piece_rank, 1)
    panels_here = panels_here.reshape(examples, piece_rank * low_rank)
    score_scale = 1.0 / (low_rank * math.sqrt(section_count))
    per_dp = asked // data_count
    owner = jnp.arange(asked) // per_dp
    meets = partners[:, owner].T == data_index
    scores = jnp.where(meets[:, :, None], mine[:, None, :] * score_scale, 0.0)
    total = section_count * data_count
    levels = list(range(total.bit_length() - 1))
    dp_levels = data_count.bit_length() - 1
    for level in levels[dp_levels:] + levels[:dp_levels]:
        route = [(i, i ^ (1 << level)) for i in range(total)]
        scores = scores + lax.ppermute(scores, ("section", "dp"), route)
    return (panels_here[None], scores)


def solution(mesh):
    placed = (
        P("dp", "mp"),
        P("section", "dp", "mp"),
        P("section", "dp", "mp"),
        P("section", "mp", "dp"),
        P("section", "mp", None),
        P("section", "mp", None),
        P("section", "dp", "mp"),
        P(),
    )
    return jax.shard_map(
        body, mesh=mesh, in_specs=placed, out_specs=(P("section", "dp", "mp"), P()), check_vma=False
    )
```

```python
import math

import jax
import jax.numpy as jnp
from jax import lax
from jax.experimental.layout import Layout, with_layout_constraint
from jax.sharding import PartitionSpec as P

LEN = 32
CHUNKS = 2


def silu_slope(pre_state):
    sigma = jax.nn.sigmoid(pre_state)
    return sigma * (1.0 + pre_state * (1.0 - sigma))


def body(cotangent, saved_inputs, pre_acts, weights, proj_in, proj_out, query_panels, partners):
    section_count = lax.axis_size("section")
    model_count = lax.axis_size("mp")
    data_count = lax.axis_size("dp")
    section_index = lax.axis_index("section")
    model_index = lax.axis_index("mp")
    data_index = lax.axis_index("dp")
    tokens = saved_inputs.shape[1]
    piece = saved_inputs.shape[2]
    length = LEN
    examples = tokens // length
    low_rank = proj_in.shape[2]
    chunk = tokens // CHUNKS
    chunk_examples = chunk // length
    top_section = section_count - 1
    piece_rank = low_rank // model_count

    w_cols = lax.all_gather(weights[0].T, "dp", axis=0, tiled=True)
    w_cols = with_layout_constraint(w_cols, Layout(major_to_minor=(0, 1)))
    slopes = silu_slope(pre_acts[0].astype(jnp.float32))
    out_proj = lax.all_gather(proj_out[0], "mp", axis=0, tiled=True)
    in_part = jnp.dot(saved_inputs[0], proj_in[0], preferred_element_type=jnp.float32)
    in_side = lax.psum(in_part, "mp")
    queries = lax.all_gather(query_panels[0], "mp", axis=1, tiled=True)
    asked = queries.shape[0] * data_count
    queries = lax.all_gather(queries, "dp", axis=0, tiled=True)

    grad_store = jnp.zeros((CHUNKS + 1, chunk, piece * model_count), jnp.bfloat16)
    outgoing = jnp.zeros((chunk, piece), jnp.bfloat16)
    is_top = section_index == top_section
    step_count = CHUNKS + section_count - 1
    for turn in range(step_count):
        chunk_at = turn - (top_section - section_index)
        active = jnp.logical_and(chunk_at >= 0, chunk_at < CHUNKS)
        clipped = jnp.clip(chunk_at, 0, CHUNKS - 1)
        row_start = clipped * chunk
        top_rows = lax.dynamic_slice_in_dim(cotangent, row_start, chunk, 0)
        if turn > 0:
            senders = [
                k for k in range(top_section + 1 - turn, top_section + 1 - turn + CHUNKS)
                if 1 <= k <= top_section
            ]
            received = lax.ppermute(outgoing, "section", [(k, k - 1) for k in senders])
            delta_piece = jnp.where(is_top, top_rows, received)
        else:
            delta_piece = top_rows
        slope_rows = lax.dynamic_slice_in_dim(slopes, row_start, chunk, 0)
        grad_piece = (delta_piece.astype(jnp.float32) * slope_rows).astype(jnp.bfloat16)
        grad_full = lax.all_gather(grad_piece, "mp", axis=1, tiled=True)
        if turn < step_count - 1:
            back_term = jnp.dot(grad_full, w_cols, preferred_element_type=jnp.float32)
            outgoing = (delta_piece.astype(jnp.float32) + back_term).astype(jnp.bfloat16)

        slot = jnp.where(active, clipped, CHUNKS)
        grad_store = lax.dynamic_update_index_in_dim(grad_store, grad_full, slot, 0)

    grads = grad_store[:CHUNKS].reshape(tokens, piece * model_count)
    out_side = jnp.dot(grads, out_proj, preferred_element_type=jnp.float32)
    whole = jnp.einsum(
        "etr,etc->erc",
        in_side.reshape(examples, length, low_rank),
        out_side.reshape(examples, length, low_rank),
        precision=lax.Precision.HIGHEST,
    ) / math.sqrt(length)
    mine = jnp.dot(
        queries, whole.reshape(examples, low_rank * low_rank).T, precision=lax.Precision.HIGHEST
    )
    panels_here = lax.dynamic_slice_in_dim(whole, model_index * piece_rank, piece_rank, 1)
    panels_here = panels_here.reshape(examples, piece_rank * low_rank)
    score_scale = 1.0 / (low_rank * math.sqrt(section_count))
    per_dp = asked // data_count
    owner = jnp.arange(asked) // per_dp
    meets = partners[:, owner].T == data_index
    scores = jnp.where(meets[:, :, None], mine[:, None, :] * score_scale, 0.0)
    total = section_count * data_count
    levels = list(range(total.bit_length() - 1))
    dp_levels = data_count.bit_length() - 1
    for level in levels[dp_levels:] + levels[:dp_levels]:
        route = [(i, i ^ (1 << level)) for i in range(total)]
        scores = scores + lax.ppermute(scores, ("section", "dp"), route)
    return (panels_here[None], scores)


def solution(mesh):
    placed = (
        P("dp", "mp"),
        P("section", "dp", "mp"),
        P("section", "dp", "mp"),
        P("section", "mp", "dp"),
        P("section", "mp", None),
        P("section", "mp", None),
        P("section", "dp", "mp"),
        P(),
    )
    return jax.shard_map(
        body, mesh=mesh, in_specs=placed, out_specs=(P("section", "dp", "mp"), P()), check_vma=False
    )
```

```python
import math

import jax
import jax.numpy as jnp
from jax import lax
from jax.experimental.layout import Layout, with_layout_constraint
from jax.sharding import PartitionSpec as P

LEN = 32
CHUNKS = 4


def silu_slope(pre_state):
    sigma = jax.nn.sigmoid(pre_state)
    return sigma * (1.0 + pre_state * (1.0 - sigma))


def body(cotangent, saved_inputs, pre_acts, weights, proj_in, proj_out, query_panels, partners):
    section_count = lax.axis_size("section")
    model_count = lax.axis_size("mp")
    data_count = lax.axis_size("dp")
    section_index = lax.axis_index("section")
    model_index = lax.axis_index("mp")
    data_index = lax.axis_index("dp")
    tokens = saved_inputs.shape[1]
    piece = saved_inputs.shape[2]
    length = LEN
    examples = tokens // length
    low_rank = proj_in.shape[2]
    chunk = tokens // CHUNKS
    chunk_examples = chunk // length
    top_section = section_count - 1
    piece_rank = low_rank // model_count

    w_cols = lax.all_gather(weights[0].T, "dp", axis=0, tiled=True)
    w_cols = with_layout_constraint(w_cols, Layout(major_to_minor=(0, 1)))
    slopes = silu_slope(pre_acts[0].astype(jnp.float32))
    out_proj = lax.all_gather(proj_out[0], "mp", axis=0, tiled=True)
    in_part = jnp.dot(saved_inputs[0], proj_in[0], preferred_element_type=jnp.float32)
    in_side = lax.psum(in_part, "mp")
    queries = lax.all_gather(query_panels[0], "mp", axis=1, tiled=True)
    asked = queries.shape[0] * data_count
    queries = lax.all_gather(queries, "dp", axis=0, tiled=True)

    grad_store = jnp.zeros((CHUNKS, chunk, piece * model_count), jnp.bfloat16)
    outgoing = jnp.zeros((chunk, piece), jnp.bfloat16)
    is_top = section_index == top_section
    step_count = CHUNKS + section_count - 1
    for turn in range(step_count):
        chunk_at = turn - (top_section - section_index)
        active = jnp.logical_and(chunk_at >= 0, chunk_at < CHUNKS)
        clipped = jnp.clip(chunk_at, 0, CHUNKS - 1)
        row_start = clipped * chunk
        top_rows = lax.dynamic_slice_in_dim(cotangent, row_start, chunk, 0)
        if turn > 0:
            senders = [
                k for k in range(top_section + 1 - turn, top_section + 1 - turn + CHUNKS)
                if 1 <= k <= top_section
            ]
            received = lax.ppermute(outgoing, "section", [(k, k - 1) for k in senders])
            delta_piece = jnp.where(is_top, top_rows, received)
        else:
            delta_piece = top_rows
        slope_rows = lax.dynamic_slice_in_dim(slopes, row_start, chunk, 0)
        grad_piece = (delta_piece.astype(jnp.float32) * slope_rows).astype(jnp.bfloat16)
        grad_full = lax.all_gather(grad_piece, "mp", axis=1, tiled=True)
        if turn < step_count - 1:
            back_term = jnp.dot(grad_full, w_cols, preferred_element_type=jnp.float32)
            outgoing = (delta_piece.astype(jnp.float32) + back_term).astype(jnp.bfloat16)

        previous = lax.dynamic_index_in_dim(grad_store, clipped, 0, keepdims=False)
        grad_store = lax.dynamic_update_index_in_dim(
            grad_store, jnp.where(active, grad_full, previous), clipped, 0
        )

    grads = grad_store.reshape(tokens, piece * model_count)
    out_side = jnp.dot(grads, out_proj, preferred_element_type=jnp.float32)
    whole = jnp.einsum(
        "etr,etc->erc",
        in_side.reshape(examples, length, low_rank),
        out_side.reshape(examples, length, low_rank),
        precision=lax.Precision.HIGHEST,
    ) / math.sqrt(length)
    mine = jnp.dot(
        queries, whole.reshape(examples, low_rank * low_rank).T, precision=lax.Precision.HIGHEST
    )
    panels_here = lax.dynamic_slice_in_dim(whole, model_index * piece_rank, piece_rank, 1)
    panels_here = panels_here.reshape(examples, piece_rank * low_rank)
    score_scale = 1.0 / (low_rank * math.sqrt(section_count))
    per_dp = asked // data_count
    owner = jnp.arange(asked) // per_dp
    meets = partners[:, owner].T == data_index
    scores = jnp.where(meets[:, :, None], mine[:, None, :] * score_scale, 0.0)
    total = section_count * data_count
    levels = list(range(total.bit_length() - 1))
    dp_levels = data_count.bit_length() - 1
    for level in levels[dp_levels:] + levels[:dp_levels]:
        route = [(i, i ^ (1 << level)) for i in range(total)]
        scores = scores + lax.ppermute(scores, ("section", "dp"), route)
    return (panels_here[None], scores)


def solution(mesh):
    placed = (
        P("dp", "mp"),
        P("section", "dp", "mp"),
        P("section", "dp", "mp"),
        P("section", "mp", "dp"),
        P("section", "mp", None),
        P("section", "mp", None),
        P("section", "dp", "mp"),
        P(),
    )
    return jax.shard_map(
        body, mesh=mesh, in_specs=placed, out_specs=(P("section", "dp", "mp"), P()), check_vma=False
    )
```

```python
import math

import jax
import jax.numpy as jnp
from jax import lax
from jax.experimental.layout import Layout, with_layout_constraint
from jax.sharding import PartitionSpec as P

LEN = 32
CHUNKS = 1


def silu_slope(pre_state):
    sigma = jax.nn.sigmoid(pre_state)
    return sigma * (1.0 + pre_state * (1.0 - sigma))


def body(cotangent, saved_inputs, pre_acts, weights, proj_in, proj_out, query_panels, partners):
    section_count = lax.axis_size("section")
    model_count = lax.axis_size("mp")
    data_count = lax.axis_size("dp")
    section_index = lax.axis_index("section")
    model_index = lax.axis_index("mp")
    data_index = lax.axis_index("dp")
    tokens = saved_inputs.shape[1]
    piece = saved_inputs.shape[2]
    length = LEN
    examples = tokens // length
    low_rank = proj_in.shape[2]
    chunk = tokens // CHUNKS
    chunk_examples = chunk // length
    top_section = section_count - 1
    piece_rank = low_rank // model_count

    w_cols = lax.all_gather(weights[0].T, "dp", axis=0, tiled=True)
    w_cols = with_layout_constraint(w_cols, Layout(major_to_minor=(0, 1)))
    slopes = silu_slope(pre_acts[0].astype(jnp.float32))
    out_proj = lax.all_gather(proj_out[0], "mp", axis=0, tiled=True)
    in_part = jnp.dot(saved_inputs[0], proj_in[0], preferred_element_type=jnp.float32)
    in_side = lax.psum(in_part, "mp")
    queries = lax.all_gather(query_panels[0], "mp", axis=1, tiled=True)
    asked = queries.shape[0] * data_count
    queries = lax.all_gather(queries, "dp", axis=0, tiled=True)

    grad_store = jnp.zeros((CHUNKS, chunk, piece * model_count), jnp.bfloat16)
    outgoing = jnp.zeros((chunk, piece), jnp.bfloat16)
    is_top = section_index == top_section
    step_count = CHUNKS + section_count - 1
    for turn in range(step_count):
        chunk_at = turn - (top_section - section_index)
        active = jnp.logical_and(chunk_at >= 0, chunk_at < CHUNKS)
        clipped = jnp.clip(chunk_at, 0, CHUNKS - 1)
        row_start = clipped * chunk
        top_rows = lax.dynamic_slice_in_dim(cotangent, row_start, chunk, 0)
        if turn > 0:
            senders = [
                k for k in range(top_section + 1 - turn, top_section + 1 - turn + CHUNKS)
                if 1 <= k <= top_section
            ]
            received = lax.ppermute(outgoing, "section", [(k, k - 1) for k in senders])
            delta_piece = jnp.where(is_top, top_rows, received)
        else:
            delta_piece = top_rows
        slope_rows = lax.dynamic_slice_in_dim(slopes, row_start, chunk, 0)
        grad_piece = (delta_piece.astype(jnp.float32) * slope_rows).astype(jnp.bfloat16)
        grad_full = lax.all_gather(grad_piece, "mp", axis=1, tiled=True)
        if turn < step_count - 1:
            back_term = jnp.dot(grad_full, w_cols, preferred_element_type=jnp.float32)
            outgoing = (delta_piece.astype(jnp.float32) + back_term).astype(jnp.bfloat16)

        previous = lax.dynamic_index_in_dim(grad_store, clipped, 0, keepdims=False)
        grad_store = lax.dynamic_update_index_in_dim(
            grad_store, jnp.where(active, grad_full, previous), clipped, 0
        )

    grads = grad_store.reshape(tokens, piece * model_count)
    out_side = jnp.dot(grads, out_proj, preferred_element_type=jnp.float32)
    whole = jnp.einsum(
        "etr,etc->erc",
        in_side.reshape(examples, length, low_rank),
        out_side.reshape(examples, length, low_rank),
        precision=lax.Precision.HIGHEST,
    ) / math.sqrt(length)
    mine = jnp.dot(
        queries, whole.reshape(examples, low_rank * low_rank).T, precision=lax.Precision.HIGHEST
    )
    panels_here = lax.dynamic_slice_in_dim(whole, model_index * piece_rank, piece_rank, 1)
    panels_here = panels_here.reshape(examples, piece_rank * low_rank)
    score_scale = 1.0 / (low_rank * math.sqrt(section_count))
    per_dp = asked // data_count
    owner = jnp.arange(asked) // per_dp
    meets = partners[:, owner].T == data_index
    scores = jnp.where(meets[:, :, None], mine[:, None, :] * score_scale, 0.0)
    total = section_count * data_count
    levels = list(range(total.bit_length() - 1))
    dp_levels = data_count.bit_length() - 1
    for level in levels[dp_levels:] + levels[:dp_levels]:
        route = [(i, i ^ (1 << level)) for i in range(total)]
        scores = scores + lax.ppermute(scores, ("section", "dp"), route)
    return (panels_here[None], scores)


def solution(mesh):
    placed = (
        P("dp", "mp"),
        P("section", "dp", "mp"),
        P("section", "dp", "mp"),
        P("section", "mp", "dp"),
        P("section", "mp", None),
        P("section", "mp", None),
        P("section", "dp", "mp"),
        P(),
    )
    return jax.shard_map(
        body, mesh=mesh, in_specs=placed, out_specs=(P("section", "dp", "mp"), P()), check_vma=False
    )
```

```python
import math

import jax
import jax.numpy as jnp
from jax import lax
from jax.experimental.layout import Layout, with_layout_constraint
from jax.sharding import PartitionSpec as P

LEN = 32
CHUNKS = 2


def silu_slope(pre_state):
    sigma = jax.nn.sigmoid(pre_state)
    return sigma * (1.0 + pre_state * (1.0 - sigma))


def body(cotangent, saved_inputs, pre_acts, weights, proj_in, proj_out, query_panels, partners):
    section_count = lax.axis_size("section")
    model_count = lax.axis_size("mp")
    data_count = lax.axis_size("dp")
    section_index = lax.axis_index("section")
    model_index = lax.axis_index("mp")
    data_index = lax.axis_index("dp")
    tokens = saved_inputs.shape[1]
    piece = saved_inputs.shape[2]
    length = LEN
    examples = tokens // length
    low_rank = proj_in.shape[2]
    chunk = tokens // CHUNKS
    chunk_examples = chunk // length
    top_section = section_count - 1
    piece_rank = low_rank // model_count

    w_cols = lax.all_gather(weights[0].T, "dp", axis=0, tiled=True)
    w_cols = with_layout_constraint(w_cols, Layout(major_to_minor=(0, 1)))
    slopes = silu_slope(pre_acts[0].astype(jnp.float32))
    out_proj = lax.all_gather(proj_out[0], "mp", axis=0, tiled=True)
    in_part = jnp.dot(saved_inputs[0], proj_in[0], preferred_element_type=jnp.float32)
    in_side = lax.psum(in_part, "mp")
    queries = lax.all_gather(query_panels[0], "mp", axis=1, tiled=True)
    asked = queries.shape[0] * data_count
    queries = lax.all_gather(queries, "dp", axis=0, tiled=True)

    grad_store = jnp.zeros((CHUNKS, chunk, piece * model_count), jnp.bfloat16)
    outgoing = jnp.zeros((chunk, piece), jnp.bfloat16)
    is_top = section_index == top_section
    step_count = CHUNKS + section_count - 1
    for turn in range(step_count):
        chunk_at = turn - (top_section - section_index)
        active = jnp.logical_and(chunk_at >= 0, chunk_at < CHUNKS)
        clipped = jnp.clip(chunk_at, 0, CHUNKS - 1)
        row_start = clipped * chunk
        top_rows = lax.dynamic_slice_in_dim(cotangent, row_start, chunk, 0)
        if turn > 0:
            senders = [
                k for k in range(top_section + 1 - turn, top_section + 1 - turn + CHUNKS)
                if 1 <= k <= top_section
            ]
            received = lax.ppermute(outgoing, "section", [(k, k - 1) for k in senders])
            delta_piece = jnp.where(is_top, top_rows, received)
        else:
            delta_piece = top_rows
        slope_rows = lax.dynamic_slice_in_dim(slopes, row_start, chunk, 0)
        grad_piece = (delta_piece.astype(jnp.float32) * slope_rows).astype(jnp.bfloat16)
        grad_full = lax.all_gather(grad_piece, "mp", axis=1, tiled=True)
        if turn < step_count - 1:
            back_term = jnp.dot(grad_full, w_cols, preferred_element_type=jnp.float32)
            outgoing = (delta_piece.astype(jnp.float32) + back_term).astype(jnp.bfloat16)

        previous = lax.dynamic_index_in_dim(grad_store, clipped, 0, keepdims=False)
        grad_store = lax.dynamic_update_index_in_dim(
            grad_store, jnp.where(active, grad_full, previous), clipped, 0
        )

    grads = grad_store.reshape(tokens, piece * model_count)
    out_side = jnp.dot(grads, out_proj, preferred_element_type=jnp.float32)
    whole = jnp.einsum(
        "etr,etc->erc",
        in_side.reshape(examples, length, low_rank),
        out_side.reshape(examples, length, low_rank),
        precision=lax.Precision.HIGHEST,
    ) / math.sqrt(length)
    mine = jnp.dot(
        queries, whole.reshape(examples, low_rank * low_rank).T, precision=lax.Precision.HIGHEST
    )
    panels_here = lax.dynamic_slice_in_dim(whole, model_index * piece_rank, piece_rank, 1)
    panels_here = panels_here.reshape(examples, piece_rank * low_rank)
    score_scale = 1.0 / (low_rank * math.sqrt(section_count))
    per_dp = asked // data_count
    owner = jnp.arange(asked) // per_dp
    meets = partners[:, owner].T == data_index
    scores = jnp.where(meets[:, :, None], mine[:, None, :] * score_scale, 0.0)
    total = section_count * data_count
    levels = list(range(total.bit_length() - 1))
    dp_levels = data_count.bit_length() - 1
    for level in levels[:dp_levels] + levels[dp_levels:]:
        route = [(i, i ^ (1 << level)) for i in range(total)]
        scores = scores + lax.ppermute(scores, ("section", "dp"), route)
    return (panels_here[None], scores)


def solution(mesh):
    placed = (
        P("dp", "mp"),
        P("section", "dp", "mp"),
        P("section", "dp", "mp"),
        P("section", "mp", "dp"),
        P("section", "mp", None),
        P("section", "mp", None),
        P("section", "dp", "mp"),
        P(),
    )
    return jax.shard_map(
        body, mesh=mesh, in_specs=placed, out_specs=(P("section", "dp", "mp"), P()), check_vma=False
    )
```
